256 devices in a mesh: dp: 8 (over z), expert: 32 (over y, x, core).
Axes of the slice: x: 4, y: 4, z: 8, core: 2. Of those that a mesh axis runs over, the one named last changes fastest.
Arguments:
- tokens: bfloat16 [32, 16, 7168], P('expert', 'dp'), may hold values from -6 to 6
- tangent: bfloat16 [32, 16, 7168], P('expert', 'dp'), may hold values from -52 to 52
- route_ids: int32 [32, 16, 8], P('expert', 'dp'), may hold values from 0 to 31, all different within a row; in each aligned block of 16 rows (0 to 15, 16 to 31, ..., all dimensions but the last counted through in order) at most 8 rows name the same one
- gate_fixed: int32 [32, 16, 8], P('expert', 'dp'), may hold values from 4096 to 65535
- gate_proj: bfloat16 [32, 7168, 2048], P('expert', None, 'dp'), may hold values from -0.0625 to 0.0625
- up_proj: bfloat16 [32, 7168, 2048], P('expert', None, 'dp'), may hold values from -0.0625 to 0.0625
- down_proj: bfloat16 [32, 2048, 7168], P('expert', 'dp'), may hold values from -0.125 to 0.125
Outputs:
- next_tangent: bfloat16 [32, 16, 7168], P('expert', 'dp')
- lipschitz: float32 [], replicated
The draws below stay inside these ranges and needn't reach their ends.
Inputs may be any that keep to these rules, and one draw needn't show every extreme that they name: `route_ids`: each token names 8 different experts; within one group of 16 tokens no expert is named by more than 8 tokens.
All inputs are finite; a program needn't handle non-finite values.
Results may differ from the reference program's by a relative error of at most 0.0065.
Values may be sent and summed in bfloat16 or wider, within the bound.
No kernel may reach another device: no remote copies, remote signals or barrier semaphores. Data moves between devices by JAX's collectives and lax.ppermute only.
A program may use at most 128 MiB of HBM per device.

```python
import math
import jax
import jax.numpy as jnp
import numpy as np
from jax import lax

D = 7168
FF = 2048
TOPK = 8
EXPERTS = 32
GROUPS = 32
GROUP_TOK = 16
TOKENS = 512
CAPC = 8


def draw_tangent(key, part):
    key_base, key_rows = jax.random.split(key, 2)
    group_pos = jnp.arange(GROUPS, dtype=jnp.float32) / max(GROUPS - 1, 1)
    token_pos = jnp.arange(GROUP_TOK, dtype=jnp.float32) / max(GROUP_TOK - 1, 1)
    rising = jnp.exp(0.5 * math.log(3.0) * (group_pos[:, None] + token_pos[None, :]))
    base = jnp.clip(jax.random.normal(key_base, (GROUPS, GROUP_TOK, D), jnp.float32), -4.0, 4.0)
    row_scale = jnp.exp(jax.random.uniform(key_rows, (GROUPS, GROUP_TOK, 1), jnp.float32, math.log(0.5), math.log(2.0)))
    return jnp.clip(base * row_scale * rising[:, :, None], -52.0, 52.0).astype(jnp.bfloat16)


def set_ends(array, own_key, smallest, largest):
    index_at = [jax.random.randint(jax.random.fold_in(own_key, axis), (), 0, length) for axis, length in enumerate(array.shape)]
    widest = array.shape.index(max(array.shape))
    next_to = index_at[:widest] + [(index_at[widest] + 1) % array.shape[widest]] + index_at[widest + 1:]
    return array.at[tuple(index_at)].set(smallest).at[tuple(next_to)].set(largest)


def block_levels(key, shape, cuts, least, largest):
    level, own = 1.0, jax.random.fold_in(key, 6)
    for dim, parts in cuts:
        draws = jnp.exp(jax.random.uniform(jax.random.fold_in(own, dim), (parts,), jnp.float32, least / len(cuts), largest / len(cuts)))
        level = level * jnp.repeat(draws, shape[dim] // parts).reshape([-1 if axis == dim else 1 for axis in range(len(shape))])
    return level


def routed_block(key, own, number, rows, count, top, bound, slope):
    order = jax.random.permutation(key, count)
    heavy_load, ordinary = portions_of(count, rows * top, bound, slope, True), portions_of(count, rows * top, bound, slope, False)
    places = jnp.arange(count)

    def named(sizes, offset_by):
        used = int((sizes > 0).sum())
        fixed = max(1, used // 4)
        passed = fixed + (places - fixed + offset_by * (used - fixed)) % max(1, count - fixed)
        return jnp.zeros((count,), jnp.int32).at[order[jnp.where(places < fixed, places, passed)]].set(jnp.asarray(sizes, jnp.int32))

    sizes = jnp.where(number % 4 == 0, named(heavy_load, number // 4), named(ordinary, number - number // 4 - 1))
    mixed = jax.random.permutation(jax.random.fold_in(own, 3), count)
    source_of, receiver = mixed[0:count // 2 * 2:2], mixed[1:count // 2 * 2:2]
    room = jnp.minimum(sizes[source_of] - 1, bound - sizes[receiver]) // 2
    room = jnp.where((source_of == order[0]) | (receiver == order[0]) | (sizes[receiver] == 0), 0, jnp.maximum(room, 0))
    passed = jax.random.randint(jax.random.fold_in(own, 4), (count // 2,), 0, 1 << 20) % (room + 1)
    sizes = sizes.at[source_of].add(-passed).at[receiver].add(passed)
    members = jnp.searchsorted(jnp.cumsum(sizes), jnp.arange(rows * top), side="right").astype(jnp.int32)
    listing = members.reshape(top, rows).T
    listing = listing[jax.random.permutation(jax.random.fold_in(own, 1), rows)]
    offset_by = jax.random.randint(jax.random.fold_in(own, 2), (rows, 1), 0, top)
    return jnp.take_along_axis(listing, (jnp.arange(top)[None, :] + offset_by) % top, axis=1)


def portions_of(number_of, total, most, lean, full):
    portions = [(1 << 20) // math.isqrt(grade ** lean) + 1 for grade in range(1, number_of + 1)]
    largest = most if full else min(most, max(-(-total // number_of), total * portions[0] // sum(portions)))
    least = 1 if total - largest >= number_of - 1 else 0
    given, surplus = [largest] + [least] * (number_of - 1), total - largest - least * (number_of - 1)
    while surplus > 0:
        candidates = [i for i in range(1, number_of) if given[i] < largest] or [i for i in range(1, number_of) if given[i] < most]
        pool, remaining = sum([portions[i] for i in candidates]), surplus
        for i in candidates:
            addition = min(most - given[i], max(1, remaining * portions[i] // pool), surplus)
            given[i] = given[i] + addition
            surplus = surplus - addition
    return np.array(given)


def normal_values(rng, shape, spread, reach, pieces=(), kind=jnp.bfloat16):
    drawn = jax.random.normal(rng, shape, jnp.float32) * spread
    if len(pieces) > 0:
        drawn = block_levels(rng, shape, pieces, -0.22, 0.18) * drawn
    return jnp.clip(drawn, min=-reach, max=reach).astype(kind)


def setup_inputs(seed: int = 0) -> dict:
    splits = jax.random.split(jax.random.key(seed), 8)
    tokens = normal_values(splits[0], (GROUPS, GROUP_TOK, D), 1.0, 6.0, ((0, 32), (1, 8)))
    tangent = draw_tangent(jax.random.fold_in(splits[7], 71), 0)
    route_ids_keys = jax.random.split(jax.random.fold_in(splits[2], 1), GROUPS * GROUP_TOK // GROUP_TOK)
    route_ids_turns = jax.random.permutation(jax.random.fold_in(splits[2], 3), GROUPS * GROUP_TOK // GROUP_TOK)
    route_ids = jax.vmap(lambda own, number: routed_block(jax.random.fold_in(splits[2], 2), own, number, GROUP_TOK, EXPERTS, TOPK, CAPC, 2))(route_ids_keys, route_ids_turns).reshape((GROUPS, GROUP_TOK, TOPK))
    gate_fixed = set_ends(jax.random.randint(splits[3], (GROUPS, GROUP_TOK, TOPK), 4096, 65536), jax.random.fold_in(splits[3], 1), 4096, 65535).astype(jnp.int32)
    gate_proj = normal_values(splits[4], (EXPERTS, D, FF), D ** -0.5, 0.0625, ((0, 32), (2, 8)))
    up_proj = normal_values(splits[5], (EXPERTS, D, FF), D ** -0.5, 0.0625, ((0, 32), (2, 8)))
    down_proj = normal_values(splits[6], (EXPERTS, FF, D), FF ** -0.5, 0.125, ((0, 32), (1, 8)))
    return dict(tokens=tokens, tangent=tangent, route_ids=route_ids, gate_fixed=gate_fixed, gate_proj=gate_proj, up_proj=up_proj, down_proj=down_proj)


def silu_parts(gate_pre):
    sigmoid_val = jax.nn.sigmoid(gate_pre)
    return (gate_pre * sigmoid_val, sigmoid_val * (1.0 + gate_pre * (1.0 - sigmoid_val)))

def contract_last(left, right):
    return lax.dot_general(left, right, (((1,), (1,)), ((), ())), preferred_element_type=jnp.float32)

def reference(tokens, tangent, route_ids, gate_fixed, gate_proj, up_proj, down_proj):
    inputs = tokens.reshape(TOKENS, D)
    probes = tangent.reshape(TOKENS, D)
    chosen_ids = route_ids.reshape(TOKENS, TOPK)
    gate_vals = gate_fixed.reshape(TOKENS, TOPK).astype(jnp.float32) / 65536.0
    token_index = jnp.arange(TOKENS, dtype=jnp.int32)

    def select_rows(expert_id):
        chosen = chosen_ids == expert_id
        weight = lax.optimization_barrier(jnp.sum(jnp.where(chosen, gate_vals, 0.0), axis=1))
        routed = jnp.any(chosen, axis=1)
        sort_keys = jnp.where(routed, token_index, token_index + TOKENS)
        picked = jnp.argsort(sort_keys, stable=True)[:GROUPS * CAPC].astype(jnp.int32)
        return (picked, jnp.where(routed[picked], weight[picked], 0.0))

    def first_pass(expert_id):
        picked, combine_coef = select_rows(expert_id)
        rows_in = inputs[picked]
        rows_dir = probes[picked]
        gate_pre = jnp.dot(rows_in, gate_proj[expert_id], preferred_element_type=jnp.float32)
        up_pre = jnp.dot(rows_in, up_proj[expert_id], preferred_element_type=jnp.float32)
        gate_dir = jnp.dot(rows_dir, gate_proj[expert_id], preferred_element_type=jnp.float32)
        up_dir = jnp.dot(rows_dir, up_proj[expert_id], preferred_element_type=jnp.float32)
        silu_value, silu_slope = silu_parts(gate_pre)
        jvp_hidden = (silu_slope * gate_dir * up_pre + silu_value * up_dir).astype(jnp.bfloat16)
        jvp_out = jnp.dot(jvp_hidden, down_proj[expert_id], preferred_element_type=jnp.float32)
        return (picked, combine_coef, jvp_out * combine_coef[:, None], silu_slope * up_pre, silu_value)
    experts_all = jnp.arange(EXPERTS, dtype=jnp.int32)
    picks, coefs, jvp_rows, coef_gate, coef_up = lax.map(first_pass, experts_all)
    product = jnp.zeros((TOKENS, D), jnp.float32).at[picks.reshape(-1)].add(jvp_rows.reshape(-1, D))
    product_bf = product.astype(jnp.bfloat16)

    def second_pass(packed):
        expert_id, picked, combine_coef, gate_coef, up_coef = packed
        grad_hidden = contract_last(product_bf[picked], down_proj[expert_id])
        grad_gate = (grad_hidden * gate_coef).astype(jnp.bfloat16)
        grad_up = (grad_hidden * up_coef).astype(jnp.bfloat16)
        vjp_out = contract_last(grad_gate, gate_proj[expert_id]) + contract_last(grad_up, up_proj[expert_id])
        return vjp_out * combine_coef[:, None]
    vjp_rows = lax.map(second_pass, (experts_all, picks, coefs, coef_gate, coef_up))
    result = jnp.zeros((TOKENS, D), jnp.float32).at[picks.reshape(-1)].add(vjp_rows.reshape(-1, D))
    probe_f = probes.astype(jnp.float32)
    probe_result = jnp.sum(probe_f * result)
    result_sq = jnp.sum(result * result)
    probe_sq = jnp.sum(probe_f * probe_f)
    next_tangent = (result * lax.rsqrt(result_sq / (TOKENS * D) + 1e-06)).astype(jnp.bfloat16)
    lipschitz = jnp.sqrt(probe_result / probe_sq)
    return (next_tangent.reshape(GROUPS, GROUP_TOK, D), lipschitz)
```

```python
import jax
import jax.numpy as jnp
from jax import lax
from jax.sharding import PartitionSpec as P

BF16 = jnp.bfloat16
F32 = jnp.float32


def silu_parts(gate_pre):
    sigmoid_val = jax.nn.sigmoid(gate_pre)
    return (gate_pre * sigmoid_val, sigmoid_val * (1.0 + gate_pre * (1.0 - sigmoid_val)))


def contract_last(left, right):
    return lax.dot_general(
        left, right, (((1,), (1,)), ((), ())), preferred_element_type=F32
    )


def exchange(value):
    return lax.all_to_all(value, "expert", split_axis=0, concat_axis=0, tiled=True)


def body(tokens, tangent, route_ids, gate_fixed, gate_proj, up_proj, down_proj):
    model_width = tokens.shape[2]
    tok_dev = tokens.shape[1]
    top_count = route_ids.shape[2]
    experts = lax.axis_size("expert")
    gates_local = gate_fixed[0]
    pieces = [
        tokens[0],
        tangent[0],
        route_ids[0].astype(BF16),
        (gates_local // 256).astype(BF16),
        (gates_local % 256).astype(BF16),
    ]
    width = 2 * model_width + 3 * top_count
    pad = (-width) % 128
    if pad:
        pieces.append(jnp.zeros((tok_dev, pad), BF16))
    packed = jnp.concatenate(pieces, axis=1)
    col = lax.all_gather(packed, "dp", axis=0, tiled=True)
    col_count = col.shape[0]
    meta = col[:, 2 * model_width: width].astype(jnp.int32)
    col_ids = meta[:, :top_count]
    col_gates = meta[:, top_count: 2 * top_count] * 256 + meta[:, 2 * top_count:]
    col_pair = jnp.concatenate(
        [col[:, :model_width], col[:, model_width: 2 * model_width]], axis=0
    )

    capacity = min(col_count, 2 * col_count * top_count // experts)
    slot_total = experts * capacity
    flat_ids = col_ids.reshape(-1)
    experts_all = jnp.arange(experts, dtype=jnp.int32)
    onehot = (flat_ids[:, None] == experts_all[None, :]).astype(jnp.int32)
    earlier = jnp.cumsum(onehot, axis=0) - onehot
    slot_place = jnp.sum(earlier * onehot, axis=1)
    target = flat_ids * capacity + slot_place
    places = jnp.arange(slot_total, dtype=jnp.int32)
    matches = target[:, None] == places[None, :]
    route_f = jnp.sum(
        matches.reshape(col_count, top_count, slot_total), axis=1
    ).astype(F32).T
    route_map = route_f.astype(BF16)
    gate_vals = col_gates.reshape(-1).astype(F32) / 65536.0
    combine_map = jnp.sum(
        jnp.where(matches, gate_vals[:, None], 0.0).reshape(col_count, top_count, slot_total),
        axis=1,
    )
    eye2 = jnp.eye(2, dtype=F32)
    pair_map = (
        route_f.reshape(experts, 1, capacity, 1, col_count)
        * eye2.reshape(1, 2, 1, 2, 1)
    ).reshape(experts * 2 * capacity, 2 * col_count).astype(BF16)
    send_pair = (
        jnp.dot(pair_map, col_pair, preferred_element_type=F32)
        .astype(BF16)
        .reshape(experts, 2 * capacity, model_width)
    )
    weight_gate = gate_proj[0]
    weight_up = up_proj[0]
    weight_down = down_proj[0]
    hidden_dev = weight_gate.shape[1]
    rows_pair = exchange(send_pair)
    groups_here = rows_pair.shape[0]
    flat_pair = rows_pair.reshape(-1, model_width)
    gate_both = jnp.dot(flat_pair, weight_gate, preferred_element_type=F32).reshape(
        groups_here, 2, capacity, hidden_dev
    )
    up_both = jnp.dot(flat_pair, weight_up, preferred_element_type=F32).reshape(
        groups_here, 2, capacity, hidden_dev
    )
    gate_pre = gate_both[:, 0].reshape(-1, hidden_dev)
    gate_dir = gate_both[:, 1].reshape(-1, hidden_dev)
    up_pre = up_both[:, 0].reshape(-1, hidden_dev)
    up_dir = up_both[:, 1].reshape(-1, hidden_dev)
    silu_value, silu_slope = silu_parts(gate_pre)
    jvp_hidden = (silu_slope * gate_dir * up_pre + silu_value * up_dir).astype(BF16)
    partial_value = jnp.dot(jvp_hidden, weight_down, preferred_element_type=F32)
    returned = exchange(
        partial_value.astype(BF16).reshape(groups_here, capacity, model_width)
    )
    gate_coef = silu_slope * up_pre
    up_coef = silu_value
    product_part = jnp.dot(
        combine_map,
        returned.reshape(slot_total, -1).astype(F32),
        precision=lax.Precision.HIGHEST,
        preferred_element_type=F32,
    )
    product_bf = lax.psum(product_part, "dp").astype(BF16)
    send_prod = (
        jnp.dot(route_map, product_bf, preferred_element_type=F32)
        .astype(BF16)
        .reshape(experts, capacity, model_width)
    )
    received = exchange(send_prod)
    grad_hidden = contract_last(received.reshape(slot_total, model_width), weight_down)
    grad_gate = (grad_hidden * gate_coef).astype(BF16)
    grad_up = (grad_hidden * up_coef).astype(BF16)
    vjp_part = contract_last(grad_gate, weight_gate) + contract_last(grad_up, weight_up)
    returned_two = exchange(
        vjp_part.astype(BF16).reshape(experts, capacity, model_width)
    )
    result_part = jnp.dot(
        combine_map,
        returned_two.reshape(slot_total, -1).astype(F32),
        precision=lax.Precision.HIGHEST,
        preferred_element_type=F32,
    )
    result = lax.psum_scatter(result_part, "dp", scatter_dimension=0, tiled=True)
    probe_f = tangent[0].astype(F32)
    probe_result, result_sq, probe_sq = lax.psum(
        (jnp.sum(probe_f * result), jnp.sum(result * result), jnp.sum(probe_f * probe_f)),
        ("dp", "expert"),
    )
    total_cells = lax.axis_size("dp") * lax.axis_size("expert") * tok_dev * model_width
    next_tangent = (result * lax.rsqrt(result_sq / total_cells + 1e-06)).astype(BF16)
    lipschitz = jnp.sqrt(probe_result / probe_sq)
    return (next_tangent[None], lipschitz)


def solution(mesh):
    return jax.shard_map(
        body,
        mesh=mesh,
        in_specs=(
            P("expert", "dp", None),
            P("expert", "dp", None),
            P("expert", "dp", None),
            P("expert", "dp", None),
            P("expert", None, "dp"),
            P("expert", None, "dp"),
            P("expert", "dp", None),
        ),
        out_specs=(P("expert", "dp", None), P()),
        check_vma=False,
    )
```

```python
import jax
import jax.numpy as jnp
from jax import lax
from jax.sharding import PartitionSpec as P

BF16 = jnp.bfloat16
F32 = jnp.float32


def silu_parts(gate_pre):
    sigmoid_val = jax.nn.sigmoid(gate_pre)
    return (gate_pre * sigmoid_val, sigmoid_val * (1.0 + gate_pre * (1.0 - sigmoid_val)))


def contract_last(left, right):
    return lax.dot_general(
        left, right, (((1,), (1,)), ((), ())), preferred_element_type=F32
    )


def exchange(value):
    return lax.all_to_all(value, "expert", split_axis=0, concat_axis=0, tiled=True)


def shifted(value, axis, size, step):
    return lax.ppermute(value, axis, [(i, (i + step) % size) for i in range(size)])


def gather_rows(value, axis):
    size = lax.axis_size(axis)
    me = lax.axis_index(axis)
    got = jnp.stack([value] + [shifted(value, axis, size, s) for s in range(1, size)])
    source_slot = (me - jnp.arange(size)) % size
    order = jnp.zeros((size,), jnp.int32).at[source_slot].set(jnp.arange(size))
    return got[order].reshape(size * value.shape[0], *value.shape[1:])


def scatter_sum_rows(value, axis):
    size = lax.axis_size(axis)
    me = lax.axis_index(axis)
    blocks = value.reshape(size, value.shape[0] // size, *value.shape[1:])
    total = lax.dynamic_index_in_dim(blocks, me, 0, keepdims=False)
    for s in range(1, size):
        outgoing = lax.dynamic_index_in_dim(blocks, (me + s) % size, 0, keepdims=False)
        total = total + shifted(outgoing, axis, size, s)
    return total


def butterfly_sum(value, axis):
    size = lax.axis_size(axis)
    step = 1
    while step < size:
        value = value + lax.ppermute(value, axis, [(i, i ^ step) for i in range(size)])
        step *= 2
    return value


def body(tokens, tangent, route_ids, gate_fixed, gate_proj, up_proj, down_proj):
    model_width = tokens.shape[2]
    tok_dev = tokens.shape[1]
    top_count = route_ids.shape[2]
    experts = lax.axis_size("expert")
    gates_local = gate_fixed[0]
    pieces = [
        tokens[0],
        tangent[0],
        route_ids[0].astype(BF16),
        (gates_local // 256).astype(BF16),
        (gates_local % 256).astype(BF16),
    ]
    width = 2 * model_width + 3 * top_count
    pad = (-width) % 128
    if pad:
        pieces.append(jnp.zeros((tok_dev, pad), BF16))
    packed = jnp.concatenate(pieces, axis=1)
    col = gather_rows(packed, "dp")
    col_count = col.shape[0]
    meta = col[:, 2 * model_width: width].astype(jnp.int32)
    col_ids = meta[:, :top_count]
    col_gates = meta[:, top_count: 2 * top_count] * 256 + meta[:, 2 * top_count:]
    col_pair = jnp.concatenate(
        [col[:, :model_width], col[:, model_width: 2 * model_width]], axis=0
    )

    capacity = min(col_count, 2 * col_count * top_count // experts)
    slot_total = experts * capacity
    flat_ids = col_ids.reshape(-1)
    experts_all = jnp.arange(experts, dtype=jnp.int32)
    onehot = (flat_ids[:, None] == experts_all[None, :]).astype(jnp.int32)
    earlier = jnp.cumsum(onehot, axis=0) - onehot
    slot_place = jnp.sum(earlier * onehot, axis=1)
    target = flat_ids * capacity + slot_place
    places = jnp.arange(slot_total, dtype=jnp.int32)
    matches = target[:, None] == places[None, :]
    route_f = jnp.sum(
        matches.reshape(col_count, top_count, slot_total), axis=1
    ).astype(F32).T
    route_map = route_f.astype(BF16)
    gate_vals = col_gates.reshape(-1).astype(F32) / 65536.0
    combine_map = jnp.sum(
        jnp.where(matches, gate_vals[:, None], 0.0).reshape(col_count, top_count, slot_total),
        axis=1,
    )
    eye2 = jnp.eye(2, dtype=F32)
    pair_map = (
        route_f.reshape(experts, 1, capacity, 1, col_count)
        * eye2.reshape(1, 2, 1, 2, 1)
    ).reshape(experts * 2 * capacity, 2 * col_count).astype(BF16)
    send_pair = (
        jnp.dot(pair_map, col_pair, preferred_element_type=F32)
        .astype(BF16)
        .reshape(experts, 2 * capacity, model_width)
    )
    weight_gate = gate_proj[0]
    weight_up = up_proj[0]
    weight_down = down_proj[0]
    hidden_dev = weight_gate.shape[1]
    rows_pair = exchange(send_pair)
    groups_here = rows_pair.shape[0]
    flat_pair = rows_pair.reshape(-1, model_width)
    gate_both = jnp.dot(flat_pair, weight_gate, preferred_element_type=F32).reshape(
        groups_here, 2, capacity, hidden_dev
    )
    up_both = jnp.dot(flat_pair, weight_up, preferred_element_type=F32).reshape(
        groups_here, 2, capacity, hidden_dev
    )
    gate_pre = gate_both[:, 0].reshape(-1, hidden_dev)
    gate_dir = gate_both[:, 1].reshape(-1, hidden_dev)
    up_pre = up_both[:, 0].reshape(-1, hidden_dev)
    up_dir = up_both[:, 1].reshape(-1, hidden_dev)
    silu_value, silu_slope = silu_parts(gate_pre)
    jvp_hidden = (silu_slope * gate_dir * up_pre + silu_value * up_dir).astype(BF16)
    partial_value = jnp.dot(jvp_hidden, weight_down, preferred_element_type=F32)
    returned = exchange(
        partial_value.astype(BF16).reshape(groups_here, capacity, model_width)
    )
    gate_coef = silu_slope * up_pre
    up_coef = silu_value
    product_part = jnp.dot(
        combine_map,
        returned.reshape(slot_total, -1).astype(F32),
        precision=lax.Precision.HIGHEST,
        preferred_element_type=F32,
    )
    product_bf = lax.psum(product_part, "dp").astype(BF16)
    send_prod = (
        jnp.dot(route_map, product_bf, preferred_element_type=F32)
        .astype(BF16)
        .reshape(experts, capacity, model_width)
    )
    received = exchange(send_prod)
    grad_hidden = contract_last(received.reshape(slot_total, model_width), weight_down)
    grad_gate = (grad_hidden * gate_coef).astype(BF16)
    grad_up = (grad_hidden * up_coef).astype(BF16)
    vjp_part = contract_last(grad_gate, weight_gate) + contract_last(grad_up, weight_up)
    returned_two = exchange(
        vjp_part.astype(BF16).reshape(experts, capacity, model_width)
    )
    result_part = jnp.dot(
        combine_map,
        returned_two.reshape(slot_total, -1).astype(F32),
        precision=lax.Precision.HIGHEST,
        preferred_element_type=F32,
    )
    result = scatter_sum_rows(result_part, "dp")
    probe_f = tangent[0].astype(F32)
    sums = jnp.stack(
        [jnp.sum(probe_f * result), jnp.sum(result * result), jnp.sum(probe_f * probe_f)]
    )
    sums = butterfly_sum(butterfly_sum(sums, "dp"), "expert")
    probe_result, result_sq, probe_sq = sums[0], sums[1], sums[2]
    total_cells = lax.axis_size("dp") * lax.axis_size("expert") * tok_dev * model_width
    next_tangent = (result * lax.rsqrt(result_sq / total_cells + 1e-06)).astype(BF16)
    lipschitz = jnp.sqrt(probe_result / probe_sq)
    return (next_tangent[None], lipschitz)


def solution(mesh):
    return jax.shard_map(
        body,
        mesh=mesh,
        in_specs=(
            P("expert", "dp", None),
            P("expert", "dp", None),
            P("expert", "dp", None),
            P("expert", "dp", None),
            P("expert", None, "dp"),
            P("expert", None, "dp"),
            P("expert", "dp", None),
        ),
        out_specs=(P("expert", "dp", None), P()),
        check_vma=False,
    )
```

```python
import jax
import jax.numpy as jnp
from jax import lax
from jax.sharding import PartitionSpec as P

BF16 = jnp.bfloat16
SIDE_COLS = 3072
F32 = jnp.float32


def silu_parts(gate_pre):
    sigmoid_val = jax.nn.sigmoid(gate_pre)
    return (gate_pre * sigmoid_val, sigmoid_val * (1.0 + gate_pre * (1.0 - sigmoid_val)))


def contract_last(left, right):
    return lax.dot_general(
        left, right, (((1,), (1,)), ((), ())), preferred_element_type=F32
    )


def exchange(value):
    return lax.all_to_all(value, "expert", split_axis=0, concat_axis=0, tiled=True)


def shifted(value, axis, size, step):
    return lax.ppermute(value, axis, [(i, (i + step) % size) for i in range(size)])


def gather_rows(value, axis):
    size = lax.axis_size(axis)
    me = lax.axis_index(axis)
    got = jnp.stack([value] + [shifted(value, axis, size, s) for s in range(1, size)])
    source_slot = (me - jnp.arange(size)) % size
    order = jnp.zeros((size,), jnp.int32).at[source_slot].set(jnp.arange(size))
    return got[order].reshape(size * value.shape[0], *value.shape[1:])


def scatter_sum_rows(value, axis):
    size = lax.axis_size(axis)
    me = lax.axis_index(axis)
    blocks = value.reshape(size, value.shape[0] // size, *value.shape[1:])
    total = lax.dynamic_index_in_dim(blocks, me, 0, keepdims=False)
    for s in range(1, size):
        outgoing = lax.dynamic_index_in_dim(blocks, (me + s) % size, 0, keepdims=False)
        total = total + shifted(outgoing, axis, size, s)
    return total


def butterfly_sum(value, axis):
    size = lax.axis_size(axis)
    step = 1
    while step < size:
        value = value + lax.ppermute(value, axis, [(i, i ^ step) for i in range(size)])
        step *= 2
    return value


def spread(send, side_cols):
    n = lax.axis_size("dp")
    me = lax.axis_index("dp")
    direct_cols = send.shape[2] - side_cols
    piece = side_cols // n
    part_b = lax.dynamic_slice_in_dim(send, direct_cols + me * piece, piece, axis=2)
    got_b = exchange(part_b)
    got_a = exchange(send[:, :, :direct_cols])
    all_b = lax.all_gather(got_b, "dp", axis=0, tiled=False)
    return got_a, all_b


def side_dot(all_b, weight_b):
    n, _, _, piece = all_b.shape
    return jnp.einsum(
        "dgrj,djh->grh", all_b, weight_b.reshape(n, piece, -1), preferred_element_type=F32
    )


def body(tokens, tangent, route_ids, gate_fixed, gate_proj, up_proj, down_proj):
    model_width = tokens.shape[2]
    tok_dev = tokens.shape[1]
    top_count = route_ids.shape[2]
    experts = lax.axis_size("expert")
    gates_local = gate_fixed[0]
    pieces = [
        tokens[0],
        tangent[0],
        route_ids[0].astype(BF16),
        (gates_local // 256).astype(BF16),
        (gates_local % 256).astype(BF16),
    ]
    width = 2 * model_width + 3 * top_count
    pad = (-width) % 128
    if pad:
        pieces.append(jnp.zeros((tok_dev, pad), BF16))
    packed = jnp.concatenate(pieces, axis=1)
    col = gather_rows(packed, "dp")
    col_count = col.shape[0]
    meta = col[:, 2 * model_width: width].astype(jnp.int32)
    col_ids = meta[:, :top_count]
    col_gates = meta[:, top_count: 2 * top_count] * 256 + meta[:, 2 * top_count:]
    col_pair = jnp.concatenate(
        [col[:, :model_width], col[:, model_width: 2 * model_width]], axis=0
    )

    capacity = min(col_count, 2 * col_count * top_count // experts)
    slot_total = experts * capacity
    flat_ids = col_ids.reshape(-1)
    experts_all = jnp.arange(experts, dtype=jnp.int32)
    onehot = (flat_ids[:, None] == experts_all[None, :]).astype(jnp.int32)
    earlier = jnp.cumsum(onehot, axis=0) - onehot
    slot_place = jnp.sum(earlier * onehot, axis=1)
    target = flat_ids * capacity + slot_place
    places = jnp.arange(slot_total, dtype=jnp.int32)
    matches = target[:, None] == places[None, :]
    route_f = jnp.sum(
        matches.reshape(col_count, top_count, slot_total), axis=1
    ).astype(F32).T
    route_map = route_f.astype(BF16)
    gate_vals = col_gates.reshape(-1).astype(F32) / 65536.0
    combine_map = jnp.sum(
        jnp.where(matches, gate_vals[:, None], 0.0).reshape(col_count, top_count, slot_total),
        axis=1,
    )
    eye2 = jnp.eye(2, dtype=F32)
    pair_map = (
        route_f.reshape(experts, 1, capacity, 1, col_count)
        * eye2.reshape(1, 2, 1, 2, 1)
    ).reshape(experts * 2 * capacity, 2 * col_count).astype(BF16)
    send_pair = (
        jnp.dot(pair_map, col_pair, preferred_element_type=F32)
        .astype(BF16)
        .reshape(experts, 2 * capacity, model_width)
    )
    weight_gate = gate_proj[0]
    weight_up = up_proj[0]
    weight_down = down_proj[0]
    hidden_dev = weight_gate.shape[1]
    side_cols = SIDE_COLS
    direct_cols = model_width - side_cols
    rows_a, rows_b = spread(send_pair, side_cols)
    groups_here = rows_a.shape[0]
    flat_a = rows_a.reshape(-1, direct_cols)
    gate_both = (
        jnp.dot(flat_a, weight_gate[:direct_cols], preferred_element_type=F32).reshape(
            groups_here, 2 * capacity, hidden_dev
        )
        + side_dot(rows_b, weight_gate[direct_cols:])
    ).reshape(groups_here, 2, capacity, hidden_dev)
    up_both = (
        jnp.dot(flat_a, weight_up[:direct_cols], preferred_element_type=F32).reshape(
            groups_here, 2 * capacity, hidden_dev
        )
        + side_dot(rows_b, weight_up[direct_cols:])
    ).reshape(groups_here, 2, capacity, hidden_dev)
    gate_pre = gate_both[:, 0].reshape(-1, hidden_dev)
    gate_dir = gate_both[:, 1].reshape(-1, hidden_dev)
    up_pre = up_both[:, 0].reshape(-1, hidden_dev)
    up_dir = up_both[:, 1].reshape(-1, hidden_dev)
    silu_value, silu_slope = silu_parts(gate_pre)
    jvp_hidden = (silu_slope * gate_dir * up_pre + silu_value * up_dir).astype(BF16)
    partial_value = jnp.dot(jvp_hidden, weight_down, preferred_element_type=F32)
    returned = exchange(
        partial_value.astype(BF16).reshape(groups_here, capacity, model_width)
    )
    gate_coef = silu_slope * up_pre
    up_coef = silu_value
    product_part = jnp.dot(
        combine_map,
        returned.reshape(slot_total, -1).astype(F32),
        precision=lax.Precision.HIGHEST,
        preferred_element_type=F32,
    )
    product_bf = lax.psum(product_part, "dp").astype(BF16)
    send_prod = (
        jnp.dot(route_map, product_bf, preferred_element_type=F32)
        .astype(BF16)
        .reshape(experts, capacity, model_width)
    )
    recv_a, recv_b = spread(send_prod, side_cols)
    grad_hidden = contract_last(
        recv_a.reshape(slot_total, direct_cols), weight_down[:, :direct_cols]
    ) + side_dot(recv_b, weight_down[:, direct_cols:].T).reshape(slot_total, hidden_dev)
    grad_gate = (grad_hidden * gate_coef).astype(BF16)
    grad_up = (grad_hidden * up_coef).astype(BF16)
    vjp_part = contract_last(grad_gate, weight_gate) + contract_last(grad_up, weight_up)
    returned_two = exchange(
        vjp_part.astype(BF16).reshape(experts, capacity, model_width)
    )
    result_part = jnp.dot(
        combine_map,
        returned_two.reshape(slot_total, -1).astype(F32),
        precision=lax.Precision.HIGHEST,
        preferred_element_type=F32,
    )
    result = scatter_sum_rows(result_part, "dp")
    probe_f = tangent[0].astype(F32)
    sums = jnp.stack(
        [jnp.sum(probe_f * result), jnp.sum(result * result), jnp.sum(probe_f * probe_f)]
    )
    sums = butterfly_sum(butterfly_sum(sums, "dp"), "expert")
    probe_result, result_sq, probe_sq = sums[0], sums[1], sums[2]
    total_cells = lax.axis_size("dp") * lax.axis_size("expert") * tok_dev * model_width
    next_tangent = (result * lax.rsqrt(result_sq / total_cells + 1e-06)).astype(BF16)
    lipschitz = jnp.sqrt(probe_result / probe_sq)
    return (next_tangent[None], lipschitz)


def solution(mesh):
    return jax.shard_map(
        body,
        mesh=mesh,
        in_specs=(
            P("expert", "dp", None),
            P("expert", "dp", None),
            P("expert", "dp", None),
            P("expert", "dp", None),
            P("expert", None, "dp"),
            P("expert", None, "dp"),
            P("expert", "dp", None),
        ),
        out_specs=(P("expert", "dp", None), P()),
        check_vma=False,
    )
```

```python
import jax
import jax.numpy as jnp
from jax import lax
from jax.sharding import PartitionSpec as P

BF16 = jnp.bfloat16
F32 = jnp.float32


def silu_parts(gate_pre):
    sigmoid_val = jax.nn.sigmoid(gate_pre)
    return (gate_pre * sigmoid_val, sigmoid_val * (1.0 + gate_pre * (1.0 - sigmoid_val)))


def contract_last(left, right):
    return lax.dot_general(
        left, right, (((1,), (1,)), ((), ())), preferred_element_type=F32
    )


def exchange(value):
    return lax.all_to_all(value, "expert", split_axis=0, concat_axis=0, tiled=True)


def shifted(value, axis, size, step):
    return lax.ppermute(value, axis, [(i, (i + step) % size) for i in range(size)])


def gather_rows(value, axis):
    size = lax.axis_size(axis)
    me = lax.axis_index(axis)
    step = 1
    while step < size:
        other = lax.ppermute(value, axis, [(i, i ^ step) for i in range(size)])
        upper = (me // step) % 2 == 1
        value = jnp.concatenate(
            [jnp.where(upper, other, value), jnp.where(upper, value, other)], axis=0
        )
        step *= 2
    return value


def scatter_sum_rows(value, axis):
    size = lax.axis_size(axis)
    me = lax.axis_index(axis)
    blocks = value.reshape(size, value.shape[0] // size, *value.shape[1:])
    total = lax.dynamic_index_in_dim(blocks, me, 0, keepdims=False)
    for s in range(1, size):
        outgoing = lax.dynamic_index_in_dim(blocks, (me + s) % size, 0, keepdims=False)
        total = total + shifted(outgoing, axis, size, s)
    return total


def butterfly_sum(value, axis):
    size = lax.axis_size(axis)
    step = 1
    while step < size:
        value = value + lax.ppermute(value, axis, [(i, i ^ step) for i in range(size)])
        step *= 2
    return value


def combine(combine_two, rows):
    both = jnp.dot(combine_two, rows, preferred_element_type=F32)
    half = both.shape[0] // 2
    return both[:half] + both[half:]


def body(tokens, tangent, route_ids, gate_fixed, gate_proj, up_proj, down_proj):
    model_width = tokens.shape[2]
    tok_dev = tokens.shape[1]
    top_count = route_ids.shape[2]
    experts = lax.axis_size("expert")
    gates_local = gate_fixed[0]
    pieces = [
        tokens[0],
        route_ids[0].astype(BF16),
        (gates_local // 256).astype(BF16),
        (gates_local % 256).astype(BF16),
    ]
    width = model_width + 3 * top_count
    pad = (-width) % 128
    if pad:
        pieces.append(jnp.zeros((tok_dev, pad), BF16))
    col = gather_rows(jnp.concatenate(pieces, axis=1), "dp")
    col_count = col.shape[0]
    meta = col[:, model_width: width].astype(jnp.int32)
    col_ids = meta[:, :top_count]
    col_gates = meta[:, top_count: 2 * top_count] * 256 + meta[:, 2 * top_count:]
    col_tokens = col[:, :model_width]
    capacity = min(col_count, 2 * col_count * top_count // experts)
    slot_total = experts * capacity
    flat_ids = col_ids.reshape(-1)
    experts_all = jnp.arange(experts, dtype=jnp.int32)
    onehot = (flat_ids[:, None] == experts_all[None, :]).astype(jnp.int32)
    earlier = jnp.cumsum(onehot, axis=0) - onehot
    slot_place = jnp.sum(earlier * onehot, axis=1)
    target = flat_ids * capacity + slot_place
    places = jnp.arange(slot_total, dtype=jnp.int32)
    matches = target[:, None] == places[None, :]
    route_f = jnp.sum(
        matches.reshape(col_count, top_count, slot_total), axis=1
    ).astype(F32).T
    route_map = route_f.astype(BF16)
    gate_vals = col_gates.reshape(-1).astype(F32) / 65536.0
    combine_map = jnp.sum(
        jnp.where(matches, gate_vals[:, None], 0.0).reshape(col_count, top_count, slot_total),
        axis=1,
    )
    combine_hi = combine_map.astype(BF16)
    combine_lo = (combine_map - combine_hi.astype(F32)).astype(BF16)
    combine_two = jnp.concatenate([combine_hi, combine_lo], axis=0)
    weight_gate = gate_proj[0]
    weight_up = up_proj[0]
    weight_down = down_proj[0]
    hidden_dev = weight_gate.shape[1]
    send_in = (
        jnp.dot(route_map, col_tokens, preferred_element_type=F32)
        .astype(BF16)
        .reshape(experts, capacity, model_width)
    )
    rows_in = exchange(send_in)
    col_tangent = gather_rows(tangent[0], "dp")
    send_dir = (
        jnp.dot(route_map, col_tangent, preferred_element_type=F32)
        .astype(BF16)
        .reshape(experts, capacity, model_width)
    )
    rows_dir = exchange(send_dir)
    groups_here = rows_in.shape[0]
    flat_in = rows_in.reshape(-1, model_width)
    flat_dir = rows_dir.reshape(-1, model_width)
    gate_pre = jnp.dot(flat_in, weight_gate, preferred_element_type=F32)
    up_pre = jnp.dot(flat_in, weight_up, preferred_element_type=F32)
    gate_dir = jnp.dot(flat_dir, weight_gate, preferred_element_type=F32)
    up_dir = jnp.dot(flat_dir, weight_up, preferred_element_type=F32)
    silu_value, silu_slope = silu_parts(gate_pre)
    jvp_hidden = (silu_slope * gate_dir * up_pre + silu_value * up_dir).astype(BF16)
    partial_value = jnp.dot(jvp_hidden, weight_down, preferred_element_type=F32)
    returned = exchange(
        partial_value.astype(BF16).reshape(groups_here, capacity, model_width)
    )
    gate_coef = silu_slope * up_pre
    up_coef = silu_value
    product_part = combine(combine_two, returned.reshape(slot_total, -1))
    product_bf = lax.psum(product_part, "dp").astype(BF16)
    send_prod = (
        jnp.dot(route_map, product_bf, preferred_element_type=F32)
        .astype(BF16)
        .reshape(experts, capacity, model_width)
    )
    received = exchange(send_prod)
    grad_hidden = contract_last(received.reshape(slot_total, model_width), weight_down)
    grad_gate = (grad_hidden * gate_coef).astype(BF16)
    grad_up = (grad_hidden * up_coef).astype(BF16)
    vjp_part = contract_last(grad_gate, weight_gate) + contract_last(grad_up, weight_up)
    returned_two = exchange(
        vjp_part.astype(BF16).reshape(experts, capacity, model_width)
    )
    result_part = combine(combine_two, returned_two.reshape(slot_total, -1))
    result = scatter_sum_rows(result_part, "dp")
    probe_f = tangent[0].astype(F32)
    sums = jnp.stack(
        [jnp.sum(probe_f * result), jnp.sum(result * result), jnp.sum(probe_f * probe_f)]
    )
    sums = butterfly_sum(butterfly_sum(sums, "dp"), "expert")
    probe_result, result_sq, probe_sq = sums[0], sums[1], sums[2]
    total_cells = lax.axis_size("dp") * lax.axis_size("expert") * tok_dev * model_width
    next_tangent = (result * lax.rsqrt(result_sq / total_cells + 1e-06)).astype(BF16)
    lipschitz = jnp.sqrt(probe_result / probe_sq)
    return (next_tangent[None], lipschitz)


def solution(mesh):
    return jax.shard_map(
        body,
        mesh=mesh,
        in_specs=(
            P("expert", "dp", None),
            P("expert", "dp", None),
            P("expert", "dp", None),
            P("expert", "dp", None),
            P("expert", None, "dp"),
            P("expert", None, "dp"),
            P("expert", "dp", None),
        ),
        out_specs=(P("expert", "dp", None), P()),
        check_vma=False,
    )
```

```python
import jax
import jax.numpy as jnp
from jax import lax
from jax.sharding import PartitionSpec as P

BF16 = jnp.bfloat16
F32 = jnp.float32


def silu_parts(gate_pre):
    sigmoid_val = jax.nn.sigmoid(gate_pre)
    return (gate_pre * sigmoid_val, sigmoid_val * (1.0 + gate_pre * (1.0 - sigmoid_val)))


def contract_last(left, right):
    return lax.dot_general(
        left, right, (((1,), (1,)), ((), ())), preferred_element_type=F32
    )


def exchange(value):
    return lax.all_to_all(value, "expert", split_axis=0, concat_axis=0, tiled=True)


def shifted(value, axis, size, step):
    return lax.ppermute(value, axis, [(i, (i + step) % size) for i in range(size)])


def gather_rows(value, axis):
    size = lax.axis_size(axis)
    me = lax.axis_index(axis)
    step = 1
    while step < size:
        other = lax.ppermute(value, axis, [(i, i ^ step) for i in range(size)])
        upper = (me // step) % 2 == 1
        value = jnp.concatenate(
            [jnp.where(upper, other, value), jnp.where(upper, value, other)], axis=0
        )
        step *= 2
    return value


def scatter_sum_rows(value, axis):
    size = lax.axis_size(axis)
    me = lax.axis_index(axis)
    blocks = value.reshape(size, value.shape[0] // size, *value.shape[1:])
    total = lax.dynamic_index_in_dim(blocks, me, 0, keepdims=False)
    for s in range(1, size):
        outgoing = lax.dynamic_index_in_dim(blocks, (me + s) % size, 0, keepdims=False)
        total = total + shifted(outgoing, axis, size, s)
    return total


def butterfly_sum(value, axis):
    size = lax.axis_size(axis)
    step = 1
    while step < size:
        value = value + lax.ppermute(value, axis, [(i, i ^ step) for i in range(size)])
        step *= 2
    return value


def combine(combine_two, rows):
    both = jnp.dot(combine_two, rows, preferred_element_type=F32)
    half = both.shape[0] // 2
    return both[:half] + both[half:]


def body(tokens, tangent, route_ids, gate_fixed, gate_proj, up_proj, down_proj):
    model_width = tokens.shape[2]
    tok_dev = tokens.shape[1]
    top_count = route_ids.shape[2]
    experts = lax.axis_size("expert")
    gates_local = gate_fixed[0]
    pieces = [
        tokens[0],
        tangent[0],
        route_ids[0].astype(BF16),
        (gates_local // 256).astype(BF16),
        (gates_local % 256).astype(BF16),
    ]
    width = 2 * model_width + 3 * top_count
    pad = (-width) % 128
    if pad:
        pieces.append(jnp.zeros((tok_dev, pad), BF16))
    packed = jnp.concatenate(pieces, axis=1)
    col = gather_rows(packed, "dp")
    col_count = col.shape[0]
    meta = col[:, 2 * model_width: width].astype(jnp.int32)
    col_ids = meta[:, :top_count]
    col_gates = meta[:, top_count: 2 * top_count] * 256 + meta[:, 2 * top_count:]
    col_pair = jnp.concatenate(
        [col[:, :model_width], col[:, model_width: 2 * model_width]], axis=0
    )

    capacity = min(col_count, 2 * col_count * top_count // experts)
    slot_total = experts * capacity
    flat_ids = col_ids.reshape(-1)
    experts_all = jnp.arange(experts, dtype=jnp.int32)
    onehot = (flat_ids[:, None] == experts_all[None, :]).astype(jnp.int32)
    earlier = jnp.cumsum(onehot, axis=0) - onehot
    slot_place = jnp.sum(earlier * onehot, axis=1)
    target = flat_ids * capacity + slot_place
    places = jnp.arange(slot_total, dtype=jnp.int32)
    matches = target[:, None] == places[None, :]
    route_f = jnp.sum(
        matches.reshape(col_count, top_count, slot_total), axis=1
    ).astype(F32).T
    route_map = route_f.astype(BF16)
    gate_vals = col_gates.reshape(-1).astype(F32) / 65536.0
    combine_map = jnp.sum(
        jnp.where(matches, gate_vals[:, None], 0.0).reshape(col_count, top_count, slot_total),
        axis=1,
    )
    combine_hi = lax.reduce_precision(combine_map, exponent_bits=8, mantissa_bits=7)
    combine_two = jnp.concatenate(
        [combine_hi.astype(BF16), (combine_map - combine_hi).astype(BF16)], axis=0
    )
    eye2 = jnp.eye(2, dtype=F32)
    pair_map = (
        route_f.reshape(experts, 1, capacity, 1, col_count)
        * eye2.reshape(1, 2, 1, 2, 1)
    ).reshape(experts * 2 * capacity, 2 * col_count).astype(BF16)
    send_pair = (
        jnp.dot(pair_map, col_pair, preferred_element_type=F32)
        .astype(BF16)
        .reshape(experts, 2 * capacity, model_width)
    )
    weight_gate = gate_proj[0]
    weight_up = up_proj[0]
    weight_down = down_proj[0]
    hidden_dev = weight_gate.shape[1]
    rows_pair = exchange(send_pair)
    groups_here = rows_pair.shape[0]
    flat_pair = rows_pair.reshape(-1, model_width)
    gate_both = jnp.dot(flat_pair, weight_gate, preferred_element_type=F32).reshape(
        groups_here, 2, capacity, hidden_dev
    )
    up_both = jnp.dot(flat_pair, weight_up, preferred_element_type=F32).reshape(
        groups_here, 2, capacity, hidden_dev
    )
    gate_pre = gate_both[:, 0].reshape(-1, hidden_dev)
    gate_dir = gate_both[:, 1].reshape(-1, hidden_dev)
    up_pre = up_both[:, 0].reshape(-1, hidden_dev)
    up_dir = up_both[:, 1].reshape(-1, hidden_dev)
    silu_value, silu_slope = silu_parts(gate_pre)
    jvp_hidden = (silu_slope * gate_dir * up_pre + silu_value * up_dir).astype(BF16)
    partial_value = jnp.dot(jvp_hidden, weight_down, preferred_element_type=F32)
    returned = exchange(
        partial_value.astype(BF16).reshape(groups_here, capacity, model_width)
    )
    gate_coef = silu_slope * up_pre
    up_coef = silu_value
    product_part = combine(combine_two, returned.reshape(slot_total, -1))
    product_bf = lax.psum(product_part, "dp").astype(BF16)
    send_prod = (
        jnp.dot(route_map, product_bf, preferred_element_type=F32)
        .astype(BF16)
        .reshape(experts, capacity, model_width)
    )
    received = exchange(send_prod)
    grad_hidden = contract_last(received.reshape(slot_total, model_width), weight_down)
    grad_gate = (grad_hidden * gate_coef).astype(BF16)
    grad_up = (grad_hidden * up_coef).astype(BF16)
    vjp_part = contract_last(grad_gate, weight_gate) + contract_last(grad_up, weight_up)
    returned_two = exchange(
        vjp_part.astype(BF16).reshape(experts, capacity, model_width)
    )
    result_part = combine(combine_two, returned_two.reshape(slot_total, -1))
    result = scatter_sum_rows(result_part, "dp")
    probe_f = tangent[0].astype(F32)
    lane = jnp.arange(128)[None, :]
    row = jnp.arange(8)[:, None] == 0
    sums = jnp.where(
        row & (lane == 0),
        jnp.sum(probe_f * result),
        jnp.where(
            row & (lane == 1),
            jnp.sum(result * result),
            jnp.where(row & (lane == 2), jnp.sum(probe_f * probe_f), 0.0),
        ),
    ).astype(F32)
    sums = butterfly_sum(butterfly_sum(sums, "dp"), "expert")
    probe_result, result_sq, probe_sq = sums[0, 0], sums[0, 1], sums[0, 2]
    total_cells = lax.axis_size("dp") * lax.axis_size("expert") * tok_dev * model_width
    next_tangent = (result * lax.rsqrt(result_sq / total_cells + 1e-06)).astype(BF16)
    lipschitz = jnp.sqrt(probe_result / probe_sq)
    return (next_tangent[None], lipschitz)


def solution(mesh):
    return jax.shard_map(
        body,
        mesh=mesh,
        in_specs=(
            P("expert", "dp", None),
            P("expert", "dp", None),
            P("expert", "dp", None),
            P("expert", "dp", None),
            P("expert", None, "dp"),
            P("expert", None, "dp"),
            P("expert", "dp", None),
        ),
        out_specs=(P("expert", "dp", None), P()),
        check_vma=False,
    )
```

```python
import jax
import jax.numpy as jnp
from jax import lax
from jax.sharding import PartitionSpec as P

BF16 = jnp.bfloat16
F32 = jnp.float32


def silu_parts(gate_pre):
    sigmoid_val = jax.nn.sigmoid(gate_pre)
    return (gate_pre * sigmoid_val, sigmoid_val * (1.0 + gate_pre * (1.0 - sigmoid_val)))


def contract_last(left, right):
    return lax.dot_general(
        left, right, (((1,), (1,)), ((), ())), preferred_element_type=F32
    )


def exchange(value):
    return lax.all_to_all(value, "expert", split_axis=0, concat_axis=0, tiled=True)


def shifted(value, axis, size, step):
    return lax.ppermute(value, axis, [(i, (i + step) % size) for i in range(size)])


def gather_rows(value, axis):
    size = lax.axis_size(axis)
    me = lax.axis_index(axis)
    got = jnp.stack([value] + [shifted(value, axis, size, s) for s in range(1, size)])
    source_slot = (me - jnp.arange(size)) % size
    order = jnp.zeros((size,), jnp.int32).at[source_slot].set(jnp.arange(size))
    return got[order].reshape(size * value.shape[0], *value.shape[1:])


def scatter_sum_rows(value, axis):
    size = lax.axis_size(axis)
    me = lax.axis_index(axis)
    blocks = value.reshape(size, value.shape[0] // size, *value.shape[1:])
    total = lax.dynamic_index_in_dim(blocks, me, 0, keepdims=False)
    for s in range(1, size):
        outgoing = lax.dynamic_index_in_dim(blocks, (me + s) % size, 0, keepdims=False)
        total = total + shifted(outgoing, axis, size, s)
    return total


def butterfly_sum(value, axis):
    size = lax.axis_size(axis)
    step = 1
    while step < size:
        value = value + lax.ppermute(value, axis, [(i, i ^ step) for i in range(size)])
        step *= 2
    return value


def combine(combine_two, rows):
    both = jnp.dot(combine_two, rows, preferred_element_type=F32)
    half = both.shape[0] // 2
    return both[:half] + both[half:]


def body(tokens, tangent, route_ids, gate_fixed, gate_proj, up_proj, down_proj):
    model_width = tokens.shape[2]
    tok_dev = tokens.shape[1]
    top_count = route_ids.shape[2]
    experts = lax.axis_size("expert")
    gates_local = gate_fixed[0]
    pieces = [
        tokens[0],
        tangent[0],
        route_ids[0].astype(BF16),
        (gates_local // 256).astype(BF16),
        (gates_local % 256).astype(BF16),
    ]
    width = 2 * model_width + 3 * top_count
    pad = (-width) % 128
    if pad:
        pieces.append(jnp.zeros((tok_dev, pad), BF16))
    packed = jnp.concatenate(pieces, axis=1)
    col = gather_rows(packed, "dp")
    col_count = col.shape[0]
    meta = col[:, 2 * model_width: width].astype(jnp.int32)
    col_ids = meta[:, :top_count]
    col_gates = meta[:, top_count: 2 * top_count] * 256 + meta[:, 2 * top_count:]
    col_pair = jnp.concatenate(
        [col[:, :model_width], col[:, model_width: 2 * model_width]], axis=0
    )

    capacity = min(col_count, 2 * col_count * top_count // experts)
    slot_total = experts * capacity
    flat_ids = col_ids.reshape(-1)
    experts_all = jnp.arange(experts, dtype=jnp.int32)
    onehot = (flat_ids[:, None] == experts_all[None, :]).astype(jnp.int32)
    earlier = jnp.cumsum(onehot, axis=0) - onehot
    slot_place = jnp.sum(earlier * onehot, axis=1)
    target = flat_ids * capacity + slot_place
    places = jnp.arange(slot_total, dtype=jnp.int32)
    matches = target[:, None] == places[None, :]
    route_f = jnp.sum(
        matches.reshape(col_count, top_count, slot_total), axis=1
    ).astype(F32).T
    route_map = route_f.astype(BF16)
    gate_vals = col_gates.reshape(-1).astype(F32) / 65536.0
    combine_map = jnp.sum(
        jnp.where(matches, gate_vals[:, None], 0.0).reshape(col_count, top_count, slot_total),
        axis=1,
    )
    combine_hi = lax.reduce_precision(combine_map, exponent_bits=8, mantissa_bits=7)
    combine_two = jnp.concatenate(
        [combine_hi.astype(BF16), (combine_map - combine_hi).astype(BF16)], axis=0
    )
    eye2 = jnp.eye(2, dtype=F32)
    pair_map = (
        route_f.reshape(experts, 1, capacity, 1, col_count)
        * eye2.reshape(1, 2, 1, 2, 1)
    ).reshape(experts * 2 * capacity, 2 * col_count).astype(BF16)
    send_pair = (
        jnp.dot(pair_map, col_pair, preferred_element_type=F32)
        .astype(BF16)
        .reshape(experts, 2 * capacity, model_width)
    )
    weight_gate = gate_proj[0]
    weight_up = up_proj[0]
    weight_down = down_proj[0]
    hidden_dev = weight_gate.shape[1]
    rows_pair = exchange(send_pair)
    groups_here = rows_pair.shape[0]
    flat_pair = rows_pair.reshape(-1, model_width)
    gate_both = jnp.dot(flat_pair, weight_gate, preferred_element_type=F32).reshape(
        groups_here, 2, capacity, hidden_dev
    )
    up_both = jnp.dot(flat_pair, weight_up, preferred_element_type=F32).reshape(
        groups_here, 2, capacity, hidden_dev
    )
    gate_pre = gate_both[:, 0].reshape(-1, hidden_dev)
    gate_dir = gate_both[:, 1].reshape(-1, hidden_dev)
    up_pre = up_both[:, 0].reshape(-1, hidden_dev)
    up_dir = up_both[:, 1].reshape(-1, hidden_dev)
    silu_value, silu_slope = silu_parts(gate_pre)
    jvp_hidden = (silu_slope * gate_dir * up_pre + silu_value * up_dir).astype(BF16)
    partial_value = jnp.dot(jvp_hidden, weight_down, preferred_element_type=F32)
    returned = exchange(
        partial_value.astype(BF16).reshape(groups_here, capacity, model_width)
    )
    gate_coef = silu_slope * up_pre
    up_coef = silu_value
    product_part = combine(combine_two, returned.reshape(slot_total, -1))
    product_bf = lax.psum(product_part, "dp").astype(BF16)
    send_prod = (
        jnp.dot(route_map, product_bf, preferred_element_type=F32)
        .astype(BF16)
        .reshape(experts, capacity, model_width)
    )
    received = exchange(send_prod)
    grad_hidden = contract_last(received.reshape(slot_total, model_width), weight_down)
    grad_gate = (grad_hidden * gate_coef).astype(BF16)
    grad_up = (grad_hidden * up_coef).astype(BF16)
    vjp_part = contract_last(grad_gate, weight_gate) + contract_last(grad_up, weight_up)
    returned_two = exchange(
        vjp_part.astype(BF16).reshape(experts, capacity, model_width)
    )
    result_part = combine(combine_two, returned_two.reshape(slot_total, -1))
    result = scatter_sum_rows(result_part, "dp")
    probe_f = tangent[0].astype(F32)
    lane = jnp.arange(128)[None, :]
    row = jnp.arange(8)[:, None] == 0
    sums = jnp.where(
        row & (lane == 0),
        jnp.sum(probe_f * result),
        jnp.where(
            row & (lane == 1),
            jnp.sum(result * result),
            jnp.where(row & (lane == 2), jnp.sum(probe_f * probe_f), 0.0),
        ),
    ).astype(F32)
    sums = butterfly_sum(butterfly_sum(lax.optimization_barrier(sums), "dp"), "expert")
    probe_result, result_sq, probe_sq = sums[0, 0], sums[0, 1], sums[0, 2]
    total_cells = lax.axis_size("dp") * lax.axis_size("expert") * tok_dev * model_width
    next_tangent = (result * lax.rsqrt(result_sq / total_cells + 1e-06)).astype(BF16)
    lipschitz = jnp.sqrt(probe_result / probe_sq)
    return (next_tangent[None], lipschitz)


def solution(mesh):
    return jax.shard_map(
        body,
        mesh=mesh,
        in_specs=(
            P("expert", "dp", None),
            P("expert", "dp", None),
            P("expert", "dp", None),
            P("expert", "dp", None),
            P("expert", None, "dp"),
            P("expert", None, "dp"),
            P("expert", "dp", None),
        ),
        out_specs=(P("expert", "dp", None), P()),
        check_vma=False,
    )
```

```python
import jax
import jax.numpy as jnp
from jax import lax
from jax.sharding import PartitionSpec as P

BF16 = jnp.bfloat16
F32 = jnp.float32


def silu_parts(gate_pre):
    sigmoid_val = jax.nn.sigmoid(gate_pre)
    return (gate_pre * sigmoid_val, sigmoid_val * (1.0 + gate_pre * (1.0 - sigmoid_val)))


def contract_last(left, right):
    return lax.dot_general(
        left, right, (((1,), (1,)), ((), ())), preferred_element_type=F32
    )


def exchange(value):
    return lax.all_to_all(value, "expert", split_axis=0, concat_axis=0, tiled=True)


def shifted(value, axis, size, step):
    return lax.ppermute(value, axis, [(i, (i + step) % size) for i in range(size)])


def gather_rows(value, axis):
    size = lax.axis_size(axis)
    copies = jnp.broadcast_to(value[None], (size,) + value.shape).reshape(
        size * value.shape[0], *value.shape[1:]
    )
    return lax.all_to_all(copies, axis, split_axis=0, concat_axis=0, tiled=True)


def scatter_sum_rows(value, axis):
    size = lax.axis_size(axis)
    got = lax.all_to_all(value, axis, split_axis=0, concat_axis=0, tiled=True)
    return jnp.sum(got.reshape(size, value.shape[0] // size, *value.shape[1:]), axis=0)


def total_sum(value, axis):
    size = lax.axis_size(axis)
    return jnp.sum(gather_rows(value, axis).reshape(size, *value.shape), axis=0)


def butterfly_sum(value, axis):
    size = lax.axis_size(axis)
    step = 1
    while step < size:
        value = value + lax.ppermute(value, axis, [(i, i ^ step) for i in range(size)])
        step *= 2
    return value


def combine(combine_two, rows):
    both = jnp.dot(combine_two, rows, preferred_element_type=F32)
    half = both.shape[0] // 2
    return both[:half] + both[half:]


def body(tokens, tangent, route_ids, gate_fixed, gate_proj, up_proj, down_proj):
    model_width = tokens.shape[2]
    tok_dev = tokens.shape[1]
    top_count = route_ids.shape[2]
    experts = lax.axis_size("expert")
    gates_local = gate_fixed[0]
    pieces = [
        tokens[0],
        tangent[0],
        route_ids[0].astype(BF16),
        (gates_local // 256).astype(BF16),
        (gates_local % 256).astype(BF16),
    ]
    width = 2 * model_width + 3 * top_count
    pad = (-width) % 128
    if pad:
        pieces.append(jnp.zeros((tok_dev, pad), BF16))
    packed = jnp.concatenate(pieces, axis=1)
    col = gather_rows(packed, "dp")
    col_count = col.shape[0]
    meta = col[:, 2 * model_width: width].astype(jnp.int32)
    col_ids = meta[:, :top_count]
    col_gates = meta[:, top_count: 2 * top_count] * 256 + meta[:, 2 * top_count:]
    col_pair = jnp.concatenate(
        [col[:, :model_width], col[:, model_width: 2 * model_width]], axis=0
    )

    capacity = min(col_count, 2 * col_count * top_count // experts)
    slot_total = experts * capacity
    flat_ids = col_ids.reshape(-1)
    experts_all = jnp.arange(experts, dtype=jnp.int32)
    onehot = (flat_ids[:, None] == experts_all[None, :]).astype(jnp.int32)
    earlier = jnp.cumsum(onehot, axis=0) - onehot
    slot_place = jnp.sum(earlier * onehot, axis=1)
    target = flat_ids * capacity + slot_place
    places = jnp.arange(slot_total, dtype=jnp.int32)
    matches = target[:, None] == places[None, :]
    route_f = jnp.sum(
        matches.reshape(col_count, top_count, slot_total), axis=1
    ).astype(F32).T
    route_map = route_f.astype(BF16)
    gate_vals = col_gates.reshape(-1).astype(F32) / 65536.0
    combine_map = jnp.sum(
        jnp.where(matches, gate_vals[:, None], 0.0).reshape(col_count, top_count, slot_total),
        axis=1,
    )
    combine_hi = lax.reduce_precision(combine_map, exponent_bits=8, mantissa_bits=7)
    combine_two = jnp.concatenate(
        [combine_hi.astype(BF16), (combine_map - combine_hi).astype(BF16)], axis=0
    )
    eye2 = jnp.eye(2, dtype=F32)
    pair_map = (
        route_f.reshape(experts, 1, capacity, 1, col_count)
        * eye2.reshape(1, 2, 1, 2, 1)
    ).reshape(experts * 2 * capacity, 2 * col_count).astype(BF16)
    send_pair = (
        jnp.dot(pair_map, col_pair, preferred_element_type=F32)
        .astype(BF16)
        .reshape(experts, 2 * capacity, model_width)
    )
    weight_gate = gate_proj[0]
    weight_up = up_proj[0]
    weight_down = down_proj[0]
    hidden_dev = weight_gate.shape[1]
    rows_pair = exchange(send_pair)
    groups_here = rows_pair.shape[0]
    flat_pair = rows_pair.reshape(-1, model_width)
    gate_both = jnp.dot(flat_pair, weight_gate, preferred_element_type=F32).reshape(
        groups_here, 2, capacity, hidden_dev
    )
    up_both = jnp.dot(flat_pair, weight_up, preferred_element_type=F32).reshape(
        groups_here, 2, capacity, hidden_dev
    )
    gate_pre = gate_both[:, 0].reshape(-1, hidden_dev)
    gate_dir = gate_both[:, 1].reshape(-1, hidden_dev)
    up_pre = up_both[:, 0].reshape(-1, hidden_dev)
    up_dir = up_both[:, 1].reshape(-1, hidden_dev)
    silu_value, silu_slope = silu_parts(gate_pre)
    jvp_hidden = (silu_slope * gate_dir * up_pre + silu_value * up_dir).astype(BF16)
    partial_value = jnp.dot(jvp_hidden, weight_down, preferred_element_type=F32)
    returned = exchange(
        partial_value.astype(BF16).reshape(groups_here, capacity, model_width)
    )
    gate_coef = silu_slope * up_pre
    up_coef = silu_value
    product_part = combine(combine_two, returned.reshape(slot_total, -1))
    product_bf = lax.psum(product_part, "dp").astype(BF16)
    send_prod = (
        jnp.dot(route_map, product_bf, preferred_element_type=F32)
        .astype(BF16)
        .reshape(experts, capacity, model_width)
    )
    received = exchange(send_prod)
    grad_hidden = contract_last(received.reshape(slot_total, model_width), weight_down)
    grad_gate = (grad_hidden * gate_coef).astype(BF16)
    grad_up = (grad_hidden * up_coef).astype(BF16)
    vjp_part = contract_last(grad_gate, weight_gate) + contract_last(grad_up, weight_up)
    returned_two = exchange(
        vjp_part.astype(BF16).reshape(experts, capacity, model_width)
    )
    result_part = combine(combine_two, returned_two.reshape(slot_total, -1))
    result = scatter_sum_rows(result_part, "dp")
    probe_f = tangent[0].astype(F32)
    lane = jnp.arange(128)[None, :]
    sums = jnp.where(
        lane == 0,
        jnp.sum(probe_f * result),
        jnp.where(
            lane == 1,
            jnp.sum(result * result),
            jnp.where(lane == 2, jnp.sum(probe_f * probe_f), 0.0),
        ),
    ).astype(F32)
    sums = total_sum(total_sum(lax.optimization_barrier(sums), "dp"), "expert")
    probe_result, result_sq, probe_sq = sums[0, 0], sums[0, 1], sums[0, 2]
    total_cells = lax.axis_size("dp") * lax.axis_size("expert") * tok_dev * model_width
    next_tangent = (result * lax.rsqrt(result_sq / total_cells + 1e-06)).astype(BF16)
    lipschitz = jnp.sqrt(probe_result / probe_sq)
    return (next_tangent[None], lipschitz)


def solution(mesh):
    return jax.shard_map(
        body,
        mesh=mesh,
        in_specs=(
            P("expert", "dp", None),
            P("expert", "dp", None),
            P("expert", "dp", None),
            P("expert", "dp", None),
            P("expert", None, "dp"),
            P("expert", None, "dp"),
            P("expert", "dp", None),
        ),
        out_specs=(P("expert", "dp", None), P()),
        check_vma=False,
    )
```

```python
import jax
import jax.numpy as jnp
from jax import lax
from jax.sharding import PartitionSpec as P

BF16 = jnp.bfloat16
F32 = jnp.float32


def silu_parts(gate_pre):
    sigmoid_val = jax.nn.sigmoid(gate_pre)
    return (gate_pre * sigmoid_val, sigmoid_val * (1.0 + gate_pre * (1.0 - sigmoid_val)))


def contract_last(left, right):
    return lax.dot_general(
        left, right, (((1,), (1,)), ((), ())), preferred_element_type=F32
    )


def exchange(value):
    return lax.all_to_all(value, "expert", split_axis=0, concat_axis=0, tiled=True)


def shifted(value, axis, size, step):
    return lax.ppermute(value, axis, [(i, (i + step) % size) for i in range(size)])


def gather_rows(value, axis):
    size = lax.axis_size(axis)
    copies = jnp.broadcast_to(value[None], (size,) + value.shape).reshape(
        size * value.shape[0], *value.shape[1:]
    )
    return lax.all_to_all(copies, axis, split_axis=0, concat_axis=0, tiled=True)


def scatter_sum_rows(value, axis):
    size = lax.axis_size(axis)
    got = lax.all_to_all(value, axis, split_axis=0, concat_axis=0, tiled=True)
    return jnp.sum(got.reshape(size, value.shape[0] // size, *value.shape[1:]), axis=0)


def total_sum(value, axis):
    size = lax.axis_size(axis)
    return jnp.sum(gather_rows(value, axis).reshape(size, *value.shape), axis=0)


def butterfly_sum(value, axis):
    size = lax.axis_size(axis)
    step = 1
    while step < size:
        value = value + lax.ppermute(value, axis, [(i, i ^ step) for i in range(size)])
        step *= 2
    return value


def combine(combine_two, rows):
    both = jnp.dot(combine_two, rows, preferred_element_type=F32)
    half = both.shape[0] // 2
    return both[:half] + both[half:]


def body(tokens, tangent, route_ids, gate_fixed, gate_proj, up_proj, down_proj):
    model_width = tokens.shape[2]
    tok_dev = tokens.shape[1]
    top_count = route_ids.shape[2]
    experts = lax.axis_size("expert")
    gates_local = gate_fixed[0]
    pieces = [
        tokens[0],
        tangent[0],
        route_ids[0].astype(BF16),
        (gates_local // 256).astype(BF16),
        (gates_local % 256).astype(BF16),
    ]
    width = 2 * model_width + 3 * top_count
    pad = (-width) % 128
    if pad:
        pieces.append(jnp.zeros((tok_dev, pad), BF16))
    packed = jnp.concatenate(pieces, axis=1)
    col = gather_rows(packed, "dp")
    col_count = col.shape[0]
    meta = col[:, 2 * model_width: width].astype(jnp.int32)
    col_ids = meta[:, :top_count]
    col_gates = meta[:, top_count: 2 * top_count] * 256 + meta[:, 2 * top_count:]
    col_pair = jnp.concatenate(
        [col[:, :model_width], col[:, model_width: 2 * model_width]], axis=0
    )

    capacity = min(col_count, 2 * col_count * top_count // experts)
    slot_total = experts * capacity
    flat_ids = col_ids.reshape(-1)
    experts_all = jnp.arange(experts, dtype=jnp.int32)
    onehot = (flat_ids[:, None] == experts_all[None, :]).astype(jnp.int32)
    earlier = jnp.cumsum(onehot, axis=0) - onehot
    slot_place = jnp.sum(earlier * onehot, axis=1)
    target = flat_ids * capacity + slot_place
    places = jnp.arange(slot_total, dtype=jnp.int32)
    matches = target[:, None] == places[None, :]
    route_f = jnp.sum(
        matches.reshape(col_count, top_count, slot_total), axis=1
    ).astype(F32).T
    route_map = route_f.astype(BF16)
    gate_vals = col_gates.reshape(-1).astype(F32) / 65536.0
    combine_map = jnp.sum(
        jnp.where(matches, gate_vals[:, None], 0.0).reshape(col_count, top_count, slot_total),
        axis=1,
    )
    combine_hi = lax.reduce_precision(combine_map, exponent_bits=8, mantissa_bits=7)
    combine_two = jnp.concatenate(
        [combine_hi.astype(BF16), (combine_map - combine_hi).astype(BF16)], axis=0
    )
    eye2 = jnp.eye(2, dtype=F32)
    pair_map = (
        route_f.reshape(experts, 1, capacity, 1, col_count)
        * eye2.reshape(1, 2, 1, 2, 1)
    ).reshape(experts * 2 * capacity, 2 * col_count).astype(BF16)
    send_pair = (
        jnp.dot(pair_map, col_pair, preferred_element_type=F32)
        .astype(BF16)
        .reshape(experts, 2 * capacity, model_width)
    )
    weight_gate = gate_proj[0]
    weight_up = up_proj[0]
    weight_down = down_proj[0]
    hidden_dev = weight_gate.shape[1]
    rows_pair = exchange(send_pair)
    groups_here = rows_pair.shape[0]
    flat_pair = rows_pair.reshape(-1, model_width)
    gate_both = jnp.dot(flat_pair, weight_gate, preferred_element_type=F32).reshape(
        groups_here, 2, capacity, hidden_dev
    )
    up_both = jnp.dot(flat_pair, weight_up, preferred_element_type=F32).reshape(
        groups_here, 2, capacity, hidden_dev
    )
    gate_pre = gate_both[:, 0].reshape(-1, hidden_dev)
    gate_dir = gate_both[:, 1].reshape(-1, hidden_dev)
    up_pre = up_both[:, 0].reshape(-1, hidden_dev)
    up_dir = up_both[:, 1].reshape(-1, hidden_dev)
    silu_value, silu_slope = silu_parts(gate_pre)
    jvp_hidden = (silu_slope * gate_dir * up_pre + silu_value * up_dir).astype(BF16)
    partial_value = jnp.dot(jvp_hidden, weight_down, preferred_element_type=F32)
    returned = exchange(
        partial_value.astype(BF16).reshape(groups_here, capacity, model_width)
    )
    gate_coef = silu_slope * up_pre
    up_coef = silu_value
    product_part = combine(combine_two, returned.reshape(slot_total, -1))
    product_bf = lax.psum(product_part, "dp").astype(BF16)
    send_prod = (
        jnp.dot(route_map, product_bf, preferred_element_type=F32)
        .astype(BF16)
        .reshape(experts, capacity, model_width)
    )
    received = exchange(send_prod)
    grad_hidden = contract_last(received.reshape(slot_total, model_width), weight_down)
    grad_gate = (grad_hidden * gate_coef).astype(BF16)
    grad_up = (grad_hidden * up_coef).astype(BF16)
    vjp_part = contract_last(grad_gate, weight_gate) + contract_last(grad_up, weight_up)
    returned_two = exchange(
        vjp_part.astype(BF16).reshape(experts, capacity, model_width)
    )
    result_part = combine(combine_two, returned_two.reshape(slot_total, -1))
    result = scatter_sum_rows(result_part, "dp")
    probe_f = tangent[0].astype(F32)
    lane = jnp.arange(128)[None, :]
    sums = jnp.where(
        lane == 0,
        jnp.sum(probe_f * result),
        jnp.where(
            lane == 1,
            jnp.sum(result * result),
            jnp.where(lane == 2, jnp.sum(probe_f * probe_f), 0.0),
        ),
    ).astype(F32)
    sums = total_sum(lax.optimization_barrier(sums), ("dp", "expert"))
    probe_result, result_sq, probe_sq = sums[0, 0], sums[0, 1], sums[0, 2]
    total_cells = lax.axis_size("dp") * lax.axis_size("expert") * tok_dev * model_width
    next_tangent = (result * lax.rsqrt(result_sq / total_cells + 1e-06)).astype(BF16)
    lipschitz = jnp.sqrt(probe_result / probe_sq)
    return (next_tangent[None], lipschitz)


def solution(mesh):
    return jax.shard_map(
        body,
        mesh=mesh,
        in_specs=(
            P("expert", "dp", None),
            P("expert", "dp", None),
            P("expert", "dp", None),
            P("expert", "dp", None),
            P("expert", None, "dp"),
            P("expert", None, "dp"),
            P("expert", "dp", None),
        ),
        out_specs=(P("expert", "dp", None), P()),
        check_vma=False,
    )
```

```python
import jax
import jax.numpy as jnp
from jax import lax
from jax.sharding import PartitionSpec as P

BF16 = jnp.bfloat16
F32 = jnp.float32


def silu_parts(gate_pre):
    sigmoid_val = jax.nn.sigmoid(gate_pre)
    return (gate_pre * sigmoid_val, sigmoid_val * (1.0 + gate_pre * (1.0 - sigmoid_val)))


def contract_last(left, right):
    return lax.dot_general(
        left, right, (((1,), (1,)), ((), ())), preferred_element_type=F32
    )


def exchange(value):
    return lax.all_to_all(value, "expert", split_axis=0, concat_axis=0, tiled=True)


def shifted(value, axis, size, step):
    return lax.ppermute(value, axis, [(i, (i + step) % size) for i in range(size)])


def gather_rows(value, axis):
    size = lax.axis_size(axis)
    copies = jnp.broadcast_to(value[None], (size,) + value.shape).reshape(
        size * value.shape[0], *value.shape[1:]
    )
    return lax.all_to_all(copies, axis, split_axis=0, concat_axis=0, tiled=True)


def scatter_sum_rows(value, axis):
    size = lax.axis_size(axis)
    got = lax.all_to_all(value.astype(BF16), axis, split_axis=0, concat_axis=0, tiled=True)
    return jnp.sum(
        got.astype(F32).reshape(size, value.shape[0] // size, *value.shape[1:]), axis=0
    )


def total_sum(value, axis):
    size = lax.axis_size(axis)
    return jnp.sum(gather_rows(value, axis).reshape(size, *value.shape), axis=0)


def butterfly_sum(value, axis):
    size = lax.axis_size(axis)
    step = 1
    while step < size:
        value = value + lax.ppermute(value, axis, [(i, i ^ step) for i in range(size)])
        step *= 2
    return value


def combine(combine_two, rows):
    both = jnp.dot(combine_two, rows, preferred_element_type=F32)
    half = both.shape[0] // 2
    return both[:half] + both[half:]


def body(tokens, tangent, route_ids, gate_fixed, gate_proj, up_proj, down_proj):
    model_width = tokens.shape[2]
    tok_dev = tokens.shape[1]
    top_count = route_ids.shape[2]
    experts = lax.axis_size("expert")
    gates_local = gate_fixed[0]
    pieces = [
        tokens[0],
        tangent[0],
        route_ids[0].astype(BF16),
        (gates_local // 256).astype(BF16),
        (gates_local % 256).astype(BF16),
    ]
    width = 2 * model_width + 3 * top_count
    pad = (-width) % 128
    if pad:
        pieces.append(jnp.zeros((tok_dev, pad), BF16))
    packed = jnp.concatenate(pieces, axis=1)
    col = gather_rows(packed, "dp")
    col_count = col.shape[0]
    meta = col[:, 2 * model_width: width].astype(jnp.int32)
    col_ids = meta[:, :top_count]
    col_gates = meta[:, top_count: 2 * top_count] * 256 + meta[:, 2 * top_count:]
    col_pair = jnp.concatenate(
        [col[:, :model_width], col[:, model_width: 2 * model_width]], axis=0
    )

    capacity = min(col_count, 2 * col_count * top_count // experts)
    slot_total = experts * capacity
    flat_ids = col_ids.reshape(-1)
    experts_all = jnp.arange(experts, dtype=jnp.int32)
    onehot = (flat_ids[:, None] == experts_all[None, :]).astype(jnp.int32)
    earlier = jnp.cumsum(onehot, axis=0) - onehot
    slot_place = jnp.sum(earlier * onehot, axis=1)
    target = flat_ids * capacity + slot_place
    places = jnp.arange(slot_total, dtype=jnp.int32)
    matches = target[:, None] == places[None, :]
    route_f = jnp.sum(
        matches.reshape(col_count, top_count, slot_total), axis=1
    ).astype(F32).T
    route_map = route_f.astype(BF16)
    gate_vals = col_gates.reshape(-1).astype(F32) / 65536.0
    combine_map = jnp.sum(
        jnp.where(matches, gate_vals[:, None], 0.0).reshape(col_count, top_count, slot_total),
        axis=1,
    )
    combine_hi = lax.reduce_precision(combine_map, exponent_bits=8, mantissa_bits=7)
    combine_two = jnp.concatenate(
        [combine_hi.astype(BF16), (combine_map - combine_hi).astype(BF16)], axis=0
    )
    eye2 = jnp.eye(2, dtype=F32)
    pair_map = (
        route_f.reshape(experts, 1, capacity, 1, col_count)
        * eye2.reshape(1, 2, 1, 2, 1)
    ).reshape(experts * 2 * capacity, 2 * col_count).astype(BF16)
    send_pair = (
        jnp.dot(pair_map, col_pair, preferred_element_type=F32)
        .astype(BF16)
        .reshape(experts, 2 * capacity, model_width)
    )
    weight_gate = gate_proj[0]
    weight_up = up_proj[0]
    weight_down = down_proj[0]
    hidden_dev = weight_gate.shape[1]
    rows_pair = exchange(send_pair)
    groups_here = rows_pair.shape[0]
    flat_pair = rows_pair.reshape(-1, model_width)
    gate_both = jnp.dot(flat_pair, weight_gate, preferred_element_type=F32).reshape(
        groups_here, 2, capacity, hidden_dev
    )
    up_both = jnp.dot(flat_pair, weight_up, preferred_element_type=F32).reshape(
        groups_here, 2, capacity, hidden_dev
    )
    gate_pre = gate_both[:, 0].reshape(-1, hidden_dev)
    gate_dir = gate_both[:, 1].reshape(-1, hidden_dev)
    up_pre = up_both[:, 0].reshape(-1, hidden_dev)
    up_dir = up_both[:, 1].reshape(-1, hidden_dev)
    silu_value, silu_slope = silu_parts(gate_pre)
    jvp_hidden = (silu_slope * gate_dir * up_pre + silu_value * up_dir).astype(BF16)
    partial_value = jnp.dot(jvp_hidden, weight_down, preferred_element_type=F32)
    returned = exchange(
        partial_value.astype(BF16).reshape(groups_here, capacity, model_width)
    )
    gate_coef = silu_slope * up_pre
    up_coef = silu_value
    product_part = combine(combine_two, returned.reshape(slot_total, -1))
    product_bf = lax.psum(product_part, "dp").astype(BF16)
    send_prod = (
        jnp.dot(route_map, product_bf, preferred_element_type=F32)
        .astype(BF16)
        .reshape(experts, capacity, model_width)
    )
    received = exchange(send_prod)
    grad_hidden = contract_last(received.reshape(slot_total, model_width), weight_down)
    grad_gate = (grad_hidden * gate_coef).astype(BF16)
    grad_up = (grad_hidden * up_coef).astype(BF16)
    vjp_part = contract_last(grad_gate, weight_gate) + contract_last(grad_up, weight_up)
    returned_two = exchange(
        vjp_part.astype(BF16).reshape(experts, capacity, model_width)
    )
    result_part = combine(combine_two, returned_two.reshape(slot_total, -1))
    result = scatter_sum_rows(result_part, "dp")
    probe_f = tangent[0].astype(F32)
    lane = jnp.arange(128)[None, :]
    sums = jnp.where(
        lane == 0,
        jnp.sum(probe_f * result),
        jnp.where(
            lane == 1,
            jnp.sum(result * result),
            jnp.where(lane == 2, jnp.sum(probe_f * probe_f), 0.0),
        ),
    ).astype(F32)
    sums = total_sum(lax.optimization_barrier(sums), ("dp", "expert"))
    probe_result, result_sq, probe_sq = sums[0, 0], sums[0, 1], sums[0, 2]
    total_cells = lax.axis_size("dp") * lax.axis_size("expert") * tok_dev * model_width
    next_tangent = (result * lax.rsqrt(result_sq / total_cells + 1e-06)).astype(BF16)
    lipschitz = jnp.sqrt(probe_result / probe_sq)
    return (next_tangent[None], lipschitz)


def solution(mesh):
    return jax.shard_map(
        body,
        mesh=mesh,
        in_specs=(
            P("expert", "dp", None),
            P("expert", "dp", None),
            P("expert", "dp", None),
            P("expert", "dp", None),
            P("expert", None, "dp"),
            P("expert", None, "dp"),
            P("expert", "dp", None),
        ),
        out_specs=(P("expert", "dp", None), P()),
        check_vma=False,
    )
```

```python
import jax
import jax.numpy as jnp
from jax import lax
from jax.sharding import PartitionSpec as P

BF16 = jnp.bfloat16
F32 = jnp.float32


def silu_parts(gate_pre):
    sigmoid_val = jax.nn.sigmoid(gate_pre)
    return (gate_pre * sigmoid_val, sigmoid_val * (1.0 + gate_pre * (1.0 - sigmoid_val)))


def contract_last(left, right):
    return lax.dot_general(
        left, right, (((1,), (1,)), ((), ())), preferred_element_type=F32
    )


def exchange(value):
    return lax.all_to_all(value, "expert", split_axis=0, concat_axis=0, tiled=True)


def shifted(value, axis, size, step):
    return lax.ppermute(value, axis, [(i, (i + step) % size) for i in range(size)])


def gather_rows(value, axis):
    size = lax.axis_size(axis)
    copies = jnp.broadcast_to(value[None], (size,) + value.shape).reshape(
        size * value.shape[0], *value.shape[1:]
    )
    return lax.all_to_all(copies, axis, split_axis=0, concat_axis=0, tiled=True)


def scatter_sum_rows(value, axis):
    size = lax.axis_size(axis)
    got = lax.all_to_all(value.astype(BF16), axis, split_axis=0, concat_axis=0, tiled=True)
    return jnp.sum(
        got.astype(F32).reshape(size, value.shape[0] // size, *value.shape[1:]), axis=0
    )


def total_sum(value, axis):
    size = lax.axis_size(axis)
    return jnp.sum(gather_rows(value, axis).reshape(size, *value.shape), axis=0)


def butterfly_sum(value, axis):
    size = lax.axis_size(axis)
    step = 1
    while step < size:
        value = value + lax.ppermute(value, axis, [(i, i ^ step) for i in range(size)])
        step *= 2
    return value


def combine(combine_two, rows):
    both = jnp.dot(combine_two, rows, preferred_element_type=F32)
    half = both.shape[0] // 2
    return both[:half] + both[half:]


def body(tokens, tangent, route_ids, gate_fixed, gate_proj, up_proj, down_proj):
    model_width = tokens.shape[2]
    tok_dev = tokens.shape[1]
    top_count = route_ids.shape[2]
    experts = lax.axis_size("expert")
    gates_local = gate_fixed[0]
    pieces = [
        tokens[0],
        tangent[0],
        route_ids[0].astype(BF16),
        (gates_local // 256).astype(BF16),
        (gates_local % 256).astype(BF16),
    ]
    width = 2 * model_width + 3 * top_count
    pad = (-width) % 128
    if pad:
        pieces.append(jnp.zeros((tok_dev, pad), BF16))
    packed = jnp.concatenate(pieces, axis=1)
    col = gather_rows(packed, "dp")
    col_count = col.shape[0]
    meta = col[:, 2 * model_width: width].astype(jnp.int32)
    col_ids = meta[:, :top_count]
    col_gates = meta[:, top_count: 2 * top_count] * 256 + meta[:, 2 * top_count:]
    col_pair = jnp.concatenate(
        [col[:, :model_width], col[:, model_width: 2 * model_width]], axis=0
    )

    capacity = min(col_count, 2 * col_count * top_count // experts)
    slot_total = experts * capacity
    flat_ids = col_ids.reshape(-1)
    experts_all = jnp.arange(experts, dtype=jnp.int32)
    onehot = (flat_ids[:, None] == experts_all[None, :]).astype(jnp.int32)
    earlier = jnp.cumsum(onehot, axis=0) - onehot
    slot_place = jnp.sum(earlier * onehot, axis=1)
    target = flat_ids * capacity + slot_place
    places = jnp.arange(slot_total, dtype=jnp.int32)
    matches = target[:, None] == places[None, :]
    route_f = jnp.sum(
        matches.reshape(col_count, top_count, slot_total), axis=1
    ).astype(F32).T
    route_map = route_f.astype(BF16)
    gate_vals = col_gates.reshape(-1).astype(F32) / 65536.0
    combine_map = jnp.sum(
        jnp.where(matches, gate_vals[:, None], 0.0).reshape(col_count, top_count, slot_total),
        axis=1,
    )
    combine_hi = lax.reduce_precision(combine_map, exponent_bits=8, mantissa_bits=7)
    combine_two = jnp.concatenate(
        [combine_hi.astype(BF16), (combine_map - combine_hi).astype(BF16)], axis=0
    )
    eye2 = jnp.eye(2, dtype=F32)
    pair_map = (
        route_f.reshape(experts, 1, capacity, 1, col_count)
        * eye2.reshape(1, 2, 1, 2, 1)
    ).reshape(experts * 2 * capacity, 2 * col_count).astype(BF16)
    send_pair = (
        jnp.dot(pair_map, col_pair, preferred_element_type=F32)
        .astype(BF16)
        .reshape(experts, 2 * capacity, model_width)
    )
    weight_gate = gate_proj[0]
    weight_up = up_proj[0]
    weight_down = down_proj[0]
    hidden_dev = weight_gate.shape[1]
    rows_pair = exchange(send_pair)
    groups_here = rows_pair.shape[0]
    flat_pair = rows_pair.reshape(-1, model_width)
    gate_both = jnp.dot(flat_pair, weight_gate, preferred_element_type=F32).reshape(
        groups_here, 2, capacity, hidden_dev
    )
    up_both = jnp.dot(flat_pair, weight_up, preferred_element_type=F32).reshape(
        groups_here, 2, capacity, hidden_dev
    )
    gate_pre = gate_both[:, 0].reshape(-1, hidden_dev)
    gate_dir = gate_both[:, 1].reshape(-1, hidden_dev)
    up_pre = up_both[:, 0].reshape(-1, hidden_dev)
    up_dir = up_both[:, 1].reshape(-1, hidden_dev)
    silu_value, silu_slope = silu_parts(gate_pre)
    jvp_hidden = (silu_slope * gate_dir * up_pre + silu_value * up_dir).astype(BF16)
    partial_value = jnp.dot(jvp_hidden, weight_down, preferred_element_type=F32)
    returned = exchange(
        partial_value.astype(BF16).reshape(groups_here, capacity, model_width)
    )
    gate_coef = silu_slope * up_pre
    up_coef = silu_value
    product_part = combine(combine_two, returned.reshape(slot_total, -1))
    product_bf = gather_rows(scatter_sum_rows(product_part, "dp").astype(BF16), "dp")
    send_prod = (
        jnp.dot(route_map, product_bf, preferred_element_type=F32)
        .astype(BF16)
        .reshape(experts, capacity, model_width)
    )
    received = exchange(send_prod)
    grad_hidden = contract_last(received.reshape(slot_total, model_width), weight_down)
    grad_gate = (grad_hidden * gate_coef).astype(BF16)
    grad_up = (grad_hidden * up_coef).astype(BF16)
    vjp_part = contract_last(grad_gate, weight_gate) + contract_last(grad_up, weight_up)
    returned_two = exchange(
        vjp_part.astype(BF16).reshape(experts, capacity, model_width)
    )
    result_part = combine(combine_two, returned_two.reshape(slot_total, -1))
    result = scatter_sum_rows(result_part, "dp")
    probe_f = tangent[0].astype(F32)
    lane = jnp.arange(128)[None, :]
    sums = jnp.where(
        lane == 0,
        jnp.sum(probe_f * result),
        jnp.where(
            lane == 1,
            jnp.sum(result * result),
            jnp.where(lane == 2, jnp.sum(probe_f * probe_f), 0.0),
        ),
    ).astype(F32)
    sums = total_sum(lax.optimization_barrier(sums), ("dp", "expert"))
    probe_result, result_sq, probe_sq = sums[0, 0], sums[0, 1], sums[0, 2]
    total_cells = lax.axis_size("dp") * lax.axis_size("expert") * tok_dev * model_width
    next_tangent = (result * lax.rsqrt(result_sq / total_cells + 1e-06)).astype(BF16)
    lipschitz = jnp.sqrt(probe_result / probe_sq)
    return (next_tangent[None], lipschitz)


def solution(mesh):
    return jax.shard_map(
        body,
        mesh=mesh,
        in_specs=(
            P("expert", "dp", None),
            P("expert", "dp", None),
            P("expert", "dp", None),
            P("expert", "dp", None),
            P("expert", None, "dp"),
            P("expert", None, "dp"),
            P("expert", "dp", None),
        ),
        out_specs=(P("expert", "dp", None), P()),
        check_vma=False,
    )
```
